256 devices in a mesh: band: 8 (over x_hi, y), dom: 32 (over x_lo, z, core).
Axes of the slice: x: 4 (x_hi: 2, x_lo: 2; x = x_hi * 2 + x_lo), y: 4, z: 8, core: 2. Of those that a mesh axis runs over, the one named last changes fastest.
Arguments:
- wave: bfloat16 [192, 19, 13, 2048], P('dom', None, None, 'band'), parts along dimension 3, may hold values from -6 to 6
- kinetic: bfloat16 [343, 343], replicated, may hold values from -1 to 1, as said below
- cell_scale: float32 [192], P('dom'), may hold values from 0.5 to 2
- potential: float32 [192, 19, 13], P('dom'), may hold values from 0.2 to 2
- proj_values: bfloat16 [512, 343], P('dom'), may hold values from -0.23925781 to 0.23925781
- piece_cell: int32 [512], P('dom'), may hold values from 0 to 5
- piece_proj: int32 [512], P('dom'), may hold values from 0 to 255
- coupling: float32 [256], replicated, may hold values from 0.5 to 2
- center: float32 [1], replicated, may hold values from 9 to 11
- halfwidth: float32 [1], replicated, may hold values from 14 to 18
Outputs:
- filtered: float32 [192, 19, 13, 2048], P('dom', None, None, 'band'), parts along dimension 3
The draws below stay inside these ranges and needn't reach their ends.
There are 8 independent parts, one for each index of `band`. The reference program is written for one: setup_inputs(seed, part) draws one part's arguments, and reference() takes and returns one part's arrays. A program takes and returns all parts, laid end to end along the dimension named above; an argument that names none is the same for every part. Nothing has to cross between parts.
Inputs may be any that keep to these rules, and one draw needn't show every extreme that they name: kinetic is symmetric.
All inputs are finite; a program needn't handle non-finite values.
Results may differ from the reference program's by a relative error of at most 0.0014.
Values may be sent and summed in bfloat16 or wider, within the bound.
No kernel may reach another device: no remote copies, remote signals or barrier semaphores. Data moves between devices by JAX's collectives and lax.ppermute only.
A program may use at most 64 MiB of HBM per device.

```python
import math
import jax
import jax.numpy as jnp
from jax import lax

P_SIZE = 7
NC = 343
CXC = 2
CYC = 3
CZC = 1
CELLS_DEV = 6
CELLS = 192
ZL = 6
ZN = 192
NYN = 19
NXN = 13
BLOCK = 128
COLS = 256
NPROJ = 256
PIECES_DEV = 16
PIECES = 512
DEGREE = 4
N_DOM = 32


def draw_kinetic(key, part):
    key_off = jax.random.fold_in(key, 11)
    key_diag = jax.random.fold_in(key, 12)
    noise_draw = jax.random.normal(key_off, (NC, NC), jnp.float32)
    symmetric = (noise_draw + noise_draw.T) * (0.02 / 1.4142135)
    diag_vals = jax.random.uniform(key_diag, (NC,), jnp.float32, minval=0.5, maxval=1.0)
    identity = jnp.eye(NC, dtype=jnp.float32)
    return (symmetric * (1.0 - identity) + identity * diag_vals[None, :]).astype(jnp.bfloat16)


def set_ends(drawn, stream_key, smallest, largest):
    spot = [jax.random.randint(jax.random.fold_in(stream_key, axis), (), 0, length) for axis, length in enumerate(drawn.shape)]
    longest = drawn.shape.index(max(drawn.shape))
    neighbour = spot[:longest] + [(spot[longest] + 1) % drawn.shape[longest]] + spot[longest + 1:]
    return drawn.at[tuple(spot)].set(smallest).at[tuple(neighbour)].set(largest)


def shard_levels(key, dims, split, low, high):
    def one(axis_at, parts):
        draws = jax.random.uniform(jax.random.fold_in(jax.random.fold_in(key, 6), axis_at), (parts,), jnp.float32, low / len(split), high / len(split))
        return jnp.repeat(jnp.exp(draws), dims[axis_at] // parts).reshape((-1,) + (1,) * (len(dims) - axis_at - 1))

    loudness = one(*split[0])
    for cut in split[1:]:
        loudness = loudness * one(*cut)
    return loudness


def noise(stream_key, extent, deviation, most, split=(), kind=jnp.bfloat16):
    values = deviation * jax.random.normal(stream_key, extent, jnp.float32)
    if split:
        values = values * shard_levels(stream_key, extent, split, -0.22, 0.18)
    return jnp.clip(values, -most, most).astype(kind)


def setup_inputs(seed: int = 0, part: int = 0) -> dict:
    streams_of = jax.random.split(jax.random.key(seed), 11)
    part_splits = jax.random.split(jax.random.fold_in(streams_of[10], part), 11)
    return {
        "wave": noise(part_splits[0], (ZN, NYN, NXN, COLS), 1.0, 6.0, ((0, 32),)),
        "kinetic": draw_kinetic(jax.random.fold_in(streams_of[10], 71), part),
        "cell_scale": jnp.clip(jnp.exp(math.log(2.0) - 1.3862944 * jax.random.uniform(streams_of[2], (CELLS,), jnp.float32) ** shard_levels(streams_of[2], (CELLS,), ((0, 32),), -0.2, 0.2)), 0.5, 2.0),
        "potential": jnp.clip(0.2 + 1.8 * jax.random.uniform(streams_of[3], (ZN, NYN, NXN), jnp.float32) ** shard_levels(streams_of[3], (ZN, NYN, NXN), ((0, 32),), -0.2, 0.2), 0.2, 2.0),
        "proj_values": noise(streams_of[4], (PIECES, NC), 0.04, 0.23925781, ((0, 32),)),
        "piece_cell": set_ends(jax.random.randint(streams_of[5], (PIECES,), 0, CELLS_DEV), jax.random.fold_in(streams_of[5], 1), 0, CELLS_DEV - 1).astype(jnp.int32),
        "piece_proj": set_ends(jax.random.randint(streams_of[6], (PIECES,), 0, NPROJ), jax.random.fold_in(streams_of[6], 1), 0, NPROJ - 1).astype(jnp.int32),
        "coupling": jnp.clip(jnp.exp(jax.random.uniform(streams_of[7], (NPROJ,), jnp.float32, math.log(0.5), math.log(2.0))), 0.5, 2.0),
        "center": jnp.clip(jax.random.uniform(streams_of[8], (1,), jnp.float32, 9.0, 11.0), 9.0, 11.0),
        "halfwidth": jnp.clip(jax.random.uniform(streams_of[9], (1,), jnp.float32, 14.0, 18.0), 14.0, 18.0),
    }


def selector(count, total_nodes):
    row_ids = jnp.arange(count * P_SIZE, dtype=jnp.int32)
    target = (row_ids // P_SIZE) * (P_SIZE - 1) + row_ids % P_SIZE
    node_ids = jnp.arange(total_nodes, dtype=jnp.int32)
    return (target[:, None] == node_ids[None, :]).astype(jnp.float32)


def extract(extended):
    pick_z = selector(CZC, extended.shape[0])
    pick_y = selector(CYC, extended.shape[1])
    pick_x = selector(CXC, extended.shape[2])
    width = extended.shape[3]
    gathered = jnp.einsum('zyxk,az,by,cx->abck', extended.astype(jnp.float32), pick_z, pick_y, pick_x,
                          precision=lax.Precision.HIGHEST)
    gathered = gathered.reshape(CZC, P_SIZE, CYC, P_SIZE, CXC, P_SIZE, width).transpose(0, 2, 4, 1, 3, 5, 6)
    return gathered.reshape(CZC * CYC * CXC, P_SIZE * P_SIZE * P_SIZE, width).astype(jnp.bfloat16)


def assemble(cell_out):
    width = cell_out.shape[2]
    grouped = cell_out.reshape(CZC, CYC, CXC, P_SIZE, P_SIZE, P_SIZE, width).transpose(0, 3, 1, 4, 2, 5, 6)
    grouped = grouped.reshape(CZC * P_SIZE, CYC * P_SIZE, CXC * P_SIZE, width)
    pick_z = selector(CZC, ZL + 1)
    pick_y = selector(CYC, NYN)
    pick_x = selector(CXC, NXN)
    return jnp.einsum('abck,az,by,cx->zyxk', grouped, pick_z, pick_y, pick_x, precision=lax.Precision.HIGHEST)


def domain_cells(rounded, domain):
    owned = lax.dynamic_slice_in_dim(rounded, (domain * ZL).astype(jnp.int32), ZL, 0)
    following = lax.dynamic_slice_in_dim(rounded, (((domain + 1) % N_DOM) * ZL).astype(jnp.int32), 1, 0)
    return extract(jnp.concatenate([owned, following], axis=0))


def apply_hamiltonian(current, kinetic, cell_scale, potential, proj_values, piece_cell, piece_proj, coupling,
                      center, halfwidth):
    width = current.shape[3]
    rounded = current.astype(jnp.bfloat16)
    domains = jnp.arange(N_DOM, dtype=jnp.int32)
    values_dom = proj_values.reshape(N_DOM, PIECES_DEV, P_SIZE * P_SIZE * P_SIZE)
    cells_dom = piece_cell.reshape(N_DOM, PIECES_DEV)
    projs_dom = piece_proj.reshape(N_DOM, PIECES_DEV)
    scales_dom = cell_scale.reshape(N_DOM, CELLS_DEV)
    proj_ids = jnp.arange(NPROJ, dtype=jnp.int32)

    def coefficient_part(items):
        domain, cell_idx, proj_idx, values = items
        cell_vals = domain_cells(rounded, domain)
        picked = jnp.take(cell_vals, cell_idx, axis=0)
        piece_coef = jnp.einsum('np,npk->nk', values.astype(jnp.float32), picked.astype(jnp.float32),
                                precision=lax.Precision.HIGHEST)
        proj_hot = (proj_idx[None, :] == proj_ids[:, None]).astype(jnp.float32)
        return jnp.dot(proj_hot, piece_coef, precision=lax.Precision.HIGHEST)

    partials = lax.map(coefficient_part, (domains, cells_dom, projs_dom, values_dom))
    summed = jnp.sum(partials, axis=0)
    scaled = (coupling[:, None] * summed).astype(jnp.bfloat16)

    def cell_part(items):
        domain, cell_idx, proj_idx, values, scales = items
        cell_vals = domain_cells(rounded, domain)
        cell_out = jnp.einsum('pq,nqk->npk', kinetic.astype(jnp.float32), cell_vals.astype(jnp.float32),
                              precision=lax.Precision.HIGHEST) * scales[:, None, None]
        proj_hot = (proj_idx[None, :] == proj_ids[:, None]).astype(jnp.float32)
        per_piece = jnp.dot(proj_hot.T, scaled.astype(jnp.float32), precision=lax.Precision.HIGHEST)
        weighted = values.astype(jnp.float32)[:, :, None] * per_piece[:, None, :]
        cell_hot = (cell_idx[None, :] == jnp.arange(CELLS_DEV, dtype=jnp.int32)[:, None]).astype(jnp.float32)
        cell_out = cell_out + jnp.einsum('mn,npk->mpk', cell_hot, weighted, precision=lax.Precision.HIGHEST)
        return assemble(cell_out)

    pieces = lax.map(cell_part, (domains, cells_dom, projs_dom, values_dom, scales_dom))
    layers = pieces[:, :ZL]
    tops = pieces[:, ZL]
    layers = layers.at[:, 0].add(jnp.roll(tops, 1, axis=0))
    applied = layers.reshape(ZN, NYN, NXN, width)
    return (applied + (potential[..., None] - center[0]) * current) / halfwidth[0]


def filter_block(block, operands):
    previous = block.astype(jnp.float32)
    current = apply_hamiltonian(previous, *operands)
    for step in range(DEGREE - 1):
        following = 2.0 * apply_hamiltonian(current, *operands) - previous
        previous = current
        current = following
    return current


def reference(wave, kinetic, cell_scale, potential, proj_values, piece_cell, piece_proj, coupling, center,
              halfwidth):
    operands = (kinetic, cell_scale, potential, proj_values, piece_cell, piece_proj, coupling, center, halfwidth)
    first = filter_block(wave[..., :BLOCK], operands)
    second = filter_block(wave[..., BLOCK:], operands)
    return jnp.concatenate([first, second], axis=3)
```

```python
import numpy as np
import jax
import jax.numpy as jnp
from jax import lax
from jax.sharding import PartitionSpec as P

P_SIZE = 7
CXC = 2
CYC = 3
CZC = 1
NPROJ = 256
DEGREE = 4

CELLS_DEV = CZC * CYC * CXC
NYN = (P_SIZE - 1) * CYC + 1
NXN = (P_SIZE - 1) * CXC + 1
FACE = P_SIZE * P_SIZE
YX = NYN * NXN
YXP = ((YX + 7) // 8) * 8
ROWS = CELLS_DEV * FACE
ROWSP = ((ROWS + 7) // 8) * 8


def face_gather():
    g = np.zeros((CELLS_DEV, FACE, YXP), np.float32)
    for cy in range(CYC):
        for cx in range(CXC):
            n = cy * CXC + cx
            for b in range(P_SIZE):
                for c in range(P_SIZE):
                    y = (P_SIZE - 1) * cy + b
                    x = (P_SIZE - 1) * cx + c
                    g[n, b * P_SIZE + c, y * NXN + x] = 1.0
    return g


def row_cells():
    idx = np.full((ROWSP,), CELLS_DEV, np.int32)
    idx[:ROWS] = np.repeat(np.arange(CELLS_DEV, dtype=np.int32), FACE)
    return idx


def passed_along(value, axis, steps):
    count = lax.axis_size(axis)
    pairs = [(source, (source + steps) % count) for source in range(count)]
    return lax.ppermute(value, axis, pairs)


def gather_axis(value, axis):
    count = lax.axis_size(axis)
    bit = 1
    while bit < count:
        pairs = [(source, source ^ bit) for source in range(count)]
        other = lax.ppermute(value, axis, pairs)
        value = jnp.concatenate([value, other], axis=0)
        bit *= 2
    return value


def local(
    wave,
    kinetic,
    cell_scale,
    potential,
    proj_values,
    piece_cell,
    piece_proj,
    coupling,
    center,
    halfwidth,
):
    zl = wave.shape[0]
    width = wave.shape[3]
    pieces = proj_values.shape[0]
    g = jnp.asarray(face_gather(), jnp.bfloat16)

    k4 = kinetic.reshape(P_SIZE, FACE, P_SIZE, FACE)
    t5 = jnp.einsum("pqzb,nbj->pnqzj", k4, g, preferred_element_type=jnp.float32)
    t5 = t5.astype(jnp.bfloat16).reshape(P_SIZE, ROWS, P_SIZE * YXP)
    t5 = jnp.pad(t5, ((0, 0), (0, ROWSP - ROWS), (0, 0)))
    tmat = t5.reshape(P_SIZE * ROWSP, P_SIZE * YXP)
    t_own = tmat[:, : zl * YXP]
    t_nb = tmat[:, zl * YXP :]

    scales = jnp.concatenate([cell_scale, jnp.zeros((1,), jnp.float32)])
    srow = jnp.take(scales, jnp.asarray(row_cells()))
    srow = jnp.tile(srow, P_SIZE)[:, None]

    gs = jnp.pad(g.reshape(ROWS, YXP), ((0, ROWSP - ROWS), (0, 0)))

    sel = (piece_cell[:, None] == jnp.arange(CELLS_DEV, dtype=jnp.int32)[None, :]).astype(jnp.bfloat16)
    gp = jnp.einsum("in,nbj->ibj", sel, g, preferred_element_type=jnp.float32).astype(jnp.bfloat16)
    pv3 = proj_values.reshape(pieces, P_SIZE, FACE)
    pglob = jnp.einsum("izb,ibj->izj", pv3, gp, preferred_element_type=jnp.float32).astype(jnp.bfloat16)
    p_own = pglob[:, :zl].reshape(pieces, zl * YXP)
    p_nb = pglob[:, zl]

    proj_all = gather_axis(piece_proj, "dom")
    match = (piece_proj[:, None] == proj_all[None, :]).astype(jnp.float32)
    couple = jnp.take(coupling, piece_proj)[:, None]

    pot = jnp.pad(potential.reshape(zl, YX), ((0, 0), (0, YXP - YX)))
    shift = (pot - center[0]).reshape(zl * YXP, 1)

    def apply_h(current):
        rounded = current.astype(jnp.bfloat16)
        neighbour = passed_along(rounded[:YXP], "dom", -1)
        piece_coef = jnp.dot(p_own, rounded, preferred_element_type=jnp.float32) + jnp.dot(
            p_nb, neighbour, preferred_element_type=jnp.float32
        )
        coef_all = gather_axis(piece_coef, "dom")
        coef = jnp.dot(match, coef_all, precision=lax.Precision.HIGHEST)
        scaled = (couple * coef).astype(jnp.bfloat16)

        kin = jnp.dot(t_own, rounded, preferred_element_type=jnp.float32) + jnp.dot(
            t_nb, neighbour, preferred_element_type=jnp.float32
        )
        cell_out = (kin * srow).reshape(P_SIZE, ROWSP, width)
        hi = cell_out.astype(jnp.bfloat16)
        lo = (cell_out - hi.astype(jnp.float32)).astype(jnp.bfloat16)
        assembled = jnp.einsum("mj,amk->ajk", gs, hi, preferred_element_type=jnp.float32) + jnp.einsum(
            "mj,amk->ajk", gs, lo, preferred_element_type=jnp.float32
        )
        nonlocal_part = jnp.einsum("izj,ik->zjk", pglob, scaled, preferred_element_type=jnp.float32)
        assembled = assembled + nonlocal_part
        shared = passed_along(assembled[-1], "dom", 1)
        applied = jnp.concatenate([(assembled[0] + shared)[None], assembled[1:-1]], axis=0)
        applied = applied.reshape(zl * YXP, width)
        return (applied + shift * current) / halfwidth[0]

    field = jnp.pad(wave.reshape(zl, YX, width), ((0, 0), (0, YXP - YX), (0, 0)))
    previous = field.reshape(zl * YXP, width).astype(jnp.float32)
    current = apply_h(previous)
    for step in range(DEGREE - 1):
        following = 2.0 * apply_h(current) - previous
        previous = current
        current = following
    out = current.reshape(zl, YXP, width)[:, :YX]
    return out.reshape(wave.shape)


def solution(mesh):
    in_specs = (
        P("dom", None, None, "band"),
        P(),
        P("dom"),
        P("dom", None, None),
        P("dom", None),
        P("dom"),
        P("dom"),
        P(),
        P(),
        P(),
    )
    out_specs = P("dom", None, None, "band")
    return jax.shard_map(local, mesh=mesh, in_specs=in_specs, out_specs=out_specs, check_vma=False)
```

```python
import numpy as np
import jax
import jax.numpy as jnp
from jax import lax
from jax.sharding import PartitionSpec as P


P_SIZE = 7
CXC = 2
CYC = 3
CZC = 1
NPROJ = 256
DEGREE = 4

CELLS_DEV = CZC * CYC * CXC
NYN = (P_SIZE - 1) * CYC + 1
NXN = (P_SIZE - 1) * CXC + 1
FACE = P_SIZE * P_SIZE
YX = NYN * NXN
YXP = ((YX + 7) // 8) * 8
ROWS = CELLS_DEV * FACE
ROWSP = ((ROWS + 7) // 8) * 8


def face_gather():
    g = np.zeros((CELLS_DEV, FACE, YXP), np.float32)
    for cy in range(CYC):
        for cx in range(CXC):
            n = cy * CXC + cx
            for b in range(P_SIZE):
                for c in range(P_SIZE):
                    y = (P_SIZE - 1) * cy + b
                    x = (P_SIZE - 1) * cx + c
                    g[n, b * P_SIZE + c, y * NXN + x] = 1.0
    return g


def row_cells():
    idx = np.full((ROWSP,), CELLS_DEV, np.int32)
    idx[:ROWS] = np.repeat(np.arange(CELLS_DEV, dtype=np.int32), FACE)
    return idx


def passed_along(value, axis, steps):
    count = lax.axis_size(axis)
    pairs = [(source, (source + steps) % count) for source in range(count)]
    return lax.ppermute(value, axis, pairs)


def gather_axis(value, axis):
    count = lax.axis_size(axis)
    bit = 1
    while bit < count:
        pairs = [(source, source ^ bit) for source in range(count)]
        other = lax.ppermute(value, axis, pairs)
        value = jnp.concatenate([value, other], axis=0)
        bit *= 2
    return value


def gather_all(value, axis):
    count = lax.axis_size(axis)
    parts = [value] + [passed_along(value, axis, steps) for steps in range(1, count)]
    return jnp.concatenate(parts, axis=0)


def local(
    wave,
    kinetic,
    cell_scale,
    potential,
    proj_values,
    piece_cell,
    piece_proj,
    coupling,
    center,
    halfwidth,
):
    zl = wave.shape[0]
    width = wave.shape[3]
    pieces = proj_values.shape[0]
    g = jnp.asarray(face_gather(), jnp.bfloat16)

    k4 = kinetic.reshape(P_SIZE, FACE, P_SIZE, FACE)
    t5 = jnp.einsum("pqzb,nbj->pnqzj", k4, g, preferred_element_type=jnp.float32)
    t5 = t5.astype(jnp.bfloat16).reshape(P_SIZE, ROWS, P_SIZE * YXP)
    t5 = jnp.pad(t5, ((0, 0), (0, ROWSP - ROWS), (0, 0)))
    tmat = t5.reshape(P_SIZE * ROWSP, P_SIZE * YXP)
    t_own = tmat[:, : zl * YXP]
    t_nb = tmat[:, zl * YXP :]

    scales = jnp.concatenate([cell_scale, jnp.zeros((1,), jnp.float32)])
    srow = jnp.take(scales, jnp.asarray(row_cells()))
    srow = jnp.tile(srow, P_SIZE)[:, None]

    gs = jnp.pad(g.reshape(ROWS, YXP), ((0, ROWSP - ROWS), (0, 0)))

    sel = (piece_cell[:, None] == jnp.arange(CELLS_DEV, dtype=jnp.int32)[None, :]).astype(jnp.bfloat16)
    gp = jnp.einsum("in,nbj->ibj", sel, g, preferred_element_type=jnp.float32).astype(jnp.bfloat16)
    pv3 = proj_values.reshape(pieces, P_SIZE, FACE)
    pglob = jnp.einsum("izb,ibj->izj", pv3, gp, preferred_element_type=jnp.float32).astype(jnp.bfloat16)
    p_own = pglob[:, :zl].reshape(pieces, zl * YXP)
    p_nb = pglob[:, zl]

    prev_pnb = passed_along(p_nb, "dom", 1)
    ids = jnp.concatenate([piece_proj, passed_along(piece_proj, "dom", 1)])
    ids_all = gather_all(ids, "dom")
    match = (ids[:, None] == ids_all[None, :]).astype(jnp.float32)
    couple = jnp.take(coupling, ids)[:, None]
    p_layers = pglob[:, :zl]

    pot = jnp.pad(potential.reshape(zl, YX), ((0, 0), (0, YXP - YX)))
    shift = (pot - center[0]).reshape(zl * YXP, 1)

    def apply_h(current):
        rounded = current.astype(jnp.bfloat16)
        first = rounded[:YXP]
        own_coef = jnp.dot(p_own, rounded, preferred_element_type=jnp.float32)
        prev_coef = jnp.dot(prev_pnb, first, preferred_element_type=jnp.float32)
        coef_all = gather_all(jnp.concatenate([own_coef, prev_coef], axis=0), "dom")
        coef = jnp.dot(match, coef_all, precision=lax.Precision.HIGHEST)
        scaled = (couple * coef).astype(jnp.bfloat16)

        neighbour = passed_along(first, "dom", -1)
        kin = jnp.dot(t_own, rounded, preferred_element_type=jnp.float32) + jnp.dot(
            t_nb, neighbour, preferred_element_type=jnp.float32
        )
        cell_out = (kin * srow).reshape(P_SIZE, ROWSP, width)
        hi = cell_out.astype(jnp.bfloat16)
        lo = (cell_out - hi.astype(jnp.float32)).astype(jnp.bfloat16)
        assembled = jnp.einsum("mj,amk->ajk", gs, hi, preferred_element_type=jnp.float32) + jnp.einsum(
            "mj,amk->ajk", gs, lo, preferred_element_type=jnp.float32
        )
        shared = passed_along(assembled[-1], "dom", 1)

        own_part = jnp.einsum("izj,ik->zjk", p_layers, scaled[:pieces], preferred_element_type=jnp.float32)
        prev_part = jnp.dot(prev_pnb.T, scaled[pieces:], preferred_element_type=jnp.float32)
        applied = assembled[:-1] + own_part
        applied = jnp.concatenate([(applied[0] + (shared + prev_part))[None], applied[1:]], axis=0)
        applied = applied.reshape(zl * YXP, width)
        return (applied + shift * current) / halfwidth[0]

    field = jnp.pad(wave.reshape(zl, YX, width), ((0, 0), (0, YXP - YX), (0, 0)))
    previous = field.reshape(zl * YXP, width).astype(jnp.float32)
    current = apply_h(previous)
    for step in range(DEGREE - 1):
        following = 2.0 * apply_h(current) - previous
        previous = current
        current = following
    out = current.reshape(zl, YXP, width)[:, :YX]
    return out.reshape(wave.shape)


def solution(mesh):
    in_specs = (
        P("dom", None, None, "band"),
        P(),
        P("dom"),
        P("dom", None, None),
        P("dom", None),
        P("dom"),
        P("dom"),
        P(),
        P(),
        P(),
    )
    out_specs = P("dom", None, None, "band")
    return jax.shard_map(local, mesh=mesh, in_specs=in_specs, out_specs=out_specs, check_vma=False)
```

```python
import numpy as np
import jax
import jax.numpy as jnp
from jax import lax
from jax.sharding import PartitionSpec as P


P_SIZE = 7
CXC = 2
CYC = 3
CZC = 1
NPROJ = 256
DEGREE = 4

CELLS_DEV = CZC * CYC * CXC
NYN = (P_SIZE - 1) * CYC + 1
NXN = (P_SIZE - 1) * CXC + 1
FACE = P_SIZE * P_SIZE
YX = NYN * NXN
YXP = ((YX + 7) // 8) * 8
ROWS = CELLS_DEV * FACE
ROWSP = ((ROWS + 7) // 8) * 8


def face_gather():
    g = np.zeros((CELLS_DEV, FACE, YXP), np.float32)
    for cy in range(CYC):
        for cx in range(CXC):
            n = cy * CXC + cx
            for b in range(P_SIZE):
                for c in range(P_SIZE):
                    y = (P_SIZE - 1) * cy + b
                    x = (P_SIZE - 1) * cx + c
                    g[n, b * P_SIZE + c, y * NXN + x] = 1.0
    return g


def row_cells():
    idx = np.full((ROWSP,), CELLS_DEV, np.int32)
    idx[:ROWS] = np.repeat(np.arange(CELLS_DEV, dtype=np.int32), FACE)
    return idx


def passed_along(value, axis, steps):
    count = lax.axis_size(axis)
    pairs = [(source, (source + steps) % count) for source in range(count)]
    return lax.ppermute(value, axis, pairs)


def gather_axis(value, axis):
    count = lax.axis_size(axis)
    bit = 1
    while bit < count:
        pairs = [(source, source ^ bit) for source in range(count)]
        other = lax.ppermute(value, axis, pairs)
        value = jnp.concatenate([value, other], axis=0)
        bit *= 2
    return value


def local(
    wave,
    kinetic,
    cell_scale,
    potential,
    proj_values,
    piece_cell,
    piece_proj,
    coupling,
    center,
    halfwidth,
):
    zl = wave.shape[0]
    width = wave.shape[3]
    pieces = proj_values.shape[0]
    g = jnp.asarray(face_gather(), jnp.bfloat16)

    k4 = kinetic.reshape(P_SIZE, FACE, P_SIZE, FACE)
    t5 = jnp.einsum("pqzb,nbj->pnqzj", k4, g, preferred_element_type=jnp.float32)
    t5 = t5.astype(jnp.bfloat16).reshape(P_SIZE, ROWS, P_SIZE * YXP)
    t5 = jnp.pad(t5, ((0, 0), (0, ROWSP - ROWS), (0, 0)))
    tmat = t5.reshape(P_SIZE * ROWSP, P_SIZE * YXP)
    t_own = tmat[:, : zl * YXP]
    t_nb = tmat[:, zl * YXP :]

    scales = jnp.concatenate([cell_scale, jnp.zeros((1,), jnp.float32)])
    srow = jnp.take(scales, jnp.asarray(row_cells()))
    srow = jnp.tile(srow, P_SIZE)[:, None]

    gs = jnp.pad(g.reshape(ROWS, YXP), ((0, ROWSP - ROWS), (0, 0)))

    sel = (piece_cell[:, None] == jnp.arange(CELLS_DEV, dtype=jnp.int32)[None, :]).astype(jnp.bfloat16)
    gp = jnp.einsum("in,nbj->ibj", sel, g, preferred_element_type=jnp.float32).astype(jnp.bfloat16)
    pv3 = proj_values.reshape(pieces, P_SIZE, FACE)
    pglob = jnp.einsum("izb,ibj->izj", pv3, gp, preferred_element_type=jnp.float32).astype(jnp.bfloat16)
    p_own = pglob[:, :zl].reshape(pieces, zl * YXP)
    p_nb = pglob[:, zl]

    prev_pnb = passed_along(p_nb, "dom", 1)
    ids = jnp.concatenate([piece_proj, passed_along(piece_proj, "dom", 1)])
    ids_all = gather_axis(ids, "dom")
    match = (ids[:, None] == ids_all[None, :]).astype(jnp.float32)
    couple = jnp.take(coupling, ids)[:, None]
    p_layers = pglob[:, :zl]

    pot = jnp.pad(potential.reshape(zl, YX), ((0, 0), (0, YXP - YX)))
    shift = (pot - center[0]).reshape(zl * YXP, 1)

    def apply_h(current):
        rounded = current.astype(jnp.bfloat16)
        first = rounded[:YXP]
        own_coef = jnp.dot(p_own, rounded, preferred_element_type=jnp.float32)
        prev_coef = jnp.dot(prev_pnb, first, preferred_element_type=jnp.float32)
        coef_all = gather_axis(jnp.concatenate([own_coef, prev_coef], axis=0), "dom")
        coef = jnp.dot(match, coef_all, precision=lax.Precision.HIGHEST)
        scaled = (couple * coef).astype(jnp.bfloat16)

        neighbour = passed_along(first, "dom", -1)
        kin = jnp.dot(t_own, rounded, preferred_element_type=jnp.float32) + jnp.dot(
            t_nb, neighbour, preferred_element_type=jnp.float32
        )
        cell_out = (kin * srow).reshape(P_SIZE, ROWSP, width)
        hi = cell_out.astype(jnp.bfloat16)
        lo = (cell_out - hi.astype(jnp.float32)).astype(jnp.bfloat16)
        assembled = jnp.einsum("mj,amk->ajk", gs, hi, preferred_element_type=jnp.float32) + jnp.einsum(
            "mj,amk->ajk", gs, lo, preferred_element_type=jnp.float32
        )
        shared = passed_along(assembled[-1], "dom", 1)

        own_part = jnp.einsum("izj,ik->zjk", p_layers, scaled[:pieces], preferred_element_type=jnp.float32)
        prev_part = jnp.dot(prev_pnb.T, scaled[pieces:], preferred_element_type=jnp.float32)
        applied = assembled[:-1] + own_part
        applied = jnp.concatenate([(applied[0] + (shared + prev_part))[None], applied[1:]], axis=0)
        applied = applied.reshape(zl * YXP, width)
        return (applied + shift * current) / halfwidth[0]

    field = jnp.pad(wave.reshape(zl, YX, width), ((0, 0), (0, YXP - YX), (0, 0)))
    previous = field.reshape(zl * YXP, width).astype(jnp.float32)
    current = apply_h(previous)
    for step in range(DEGREE - 1):
        following = 2.0 * apply_h(current) - previous
        previous = current
        current = following
    out = current.reshape(zl, YXP, width)[:, :YX]
    return out.reshape(wave.shape)


def solution(mesh):
    in_specs = (
        P("dom", None, None, "band"),
        P(),
        P("dom"),
        P("dom", None, None),
        P("dom", None),
        P("dom"),
        P("dom"),
        P(),
        P(),
        P(),
    )
    out_specs = P("dom", None, None, "band")
    return jax.shard_map(local, mesh=mesh, in_specs=in_specs, out_specs=out_specs, check_vma=False)
```

```python
import numpy as np
import jax
import jax.numpy as jnp
from jax import lax
from jax.sharding import PartitionSpec as P


P_SIZE = 7
CXC = 2
CYC = 3
CZC = 1
NPROJ = 256
DEGREE = 4

CELLS_DEV = CZC * CYC * CXC
NYN = (P_SIZE - 1) * CYC + 1
NXN = (P_SIZE - 1) * CXC + 1
FACE = P_SIZE * P_SIZE
YX = NYN * NXN
YXP = ((YX + 7) // 8) * 8
ROWS = CELLS_DEV * FACE
ROWSP = ((ROWS + 7) // 8) * 8


def face_gather():
    g = np.zeros((CELLS_DEV, FACE, YXP), np.float32)
    for cy in range(CYC):
        for cx in range(CXC):
            n = cy * CXC + cx
            for b in range(P_SIZE):
                for c in range(P_SIZE):
                    y = (P_SIZE - 1) * cy + b
                    x = (P_SIZE - 1) * cx + c
                    g[n, b * P_SIZE + c, y * NXN + x] = 1.0
    return g


def row_cells():
    idx = np.full((ROWSP,), CELLS_DEV, np.int32)
    idx[:ROWS] = np.repeat(np.arange(CELLS_DEV, dtype=np.int32), FACE)
    return idx


def passed_along(value, axis, steps):
    count = lax.axis_size(axis)
    pairs = [(source, (source + steps) % count) for source in range(count)]
    return lax.ppermute(value, axis, pairs)


def gather_axis(value, axis):
    count = lax.axis_size(axis)
    bit = count // 2
    while bit >= 1:
        pairs = [(source, source ^ bit) for source in range(count)]
        other = lax.ppermute(value, axis, pairs)
        value = jnp.concatenate([value, other], axis=0)
        bit //= 2
    return value


def local(
    wave,
    kinetic,
    cell_scale,
    potential,
    proj_values,
    piece_cell,
    piece_proj,
    coupling,
    center,
    halfwidth,
):
    zl = wave.shape[0]
    width = wave.shape[3]
    pieces = proj_values.shape[0]
    g = jnp.asarray(face_gather(), jnp.bfloat16)

    k4 = kinetic.reshape(P_SIZE, FACE, P_SIZE, FACE)
    t5 = jnp.einsum("pqzb,nbj->pnqzj", k4, g, preferred_element_type=jnp.float32)
    t5 = t5.astype(jnp.bfloat16).reshape(P_SIZE, ROWS, P_SIZE * YXP)
    t5 = jnp.pad(t5, ((0, 0), (0, ROWSP - ROWS), (0, 0)))
    tmat = t5.reshape(P_SIZE * ROWSP, P_SIZE * YXP)
    t_own = tmat[:, : zl * YXP]
    t_nb = tmat[:, zl * YXP :]

    scales = jnp.concatenate([cell_scale, jnp.zeros((1,), jnp.float32)])
    srow = jnp.take(scales, jnp.asarray(row_cells()))
    srow = jnp.tile(srow, P_SIZE)[:, None]

    gs = jnp.pad(g.reshape(ROWS, YXP), ((0, ROWSP - ROWS), (0, 0)))

    sel = (piece_cell[:, None] == jnp.arange(CELLS_DEV, dtype=jnp.int32)[None, :]).astype(jnp.bfloat16)
    gp = jnp.einsum("in,nbj->ibj", sel, g, preferred_element_type=jnp.float32).astype(jnp.bfloat16)
    pv3 = proj_values.reshape(pieces, P_SIZE, FACE)
    pglob = jnp.einsum("izb,ibj->izj", pv3, gp, preferred_element_type=jnp.float32).astype(jnp.bfloat16)
    p_own = pglob[:, :zl].reshape(pieces, zl * YXP)
    p_nb = pglob[:, zl]

    prev_pnb = passed_along(p_nb, "dom", 1)
    ids = jnp.concatenate([piece_proj, passed_along(piece_proj, "dom", 1)])
    ids_all = gather_axis(piece_proj, "dom")
    match = (ids[:, None] == ids_all[None, :]).astype(jnp.float32)
    couple = jnp.take(coupling, ids)[:, None]
    p_layers = pglob[:, :zl]

    pot = jnp.pad(potential.reshape(zl, YX), ((0, 0), (0, YXP - YX)))
    shift = (pot - center[0]).reshape(zl * YXP, 1)

    def apply_h(current):
        rounded = current.astype(jnp.bfloat16)
        first = rounded[:YXP]
        own_coef = jnp.dot(p_own, rounded, preferred_element_type=jnp.float32)
        prev_coef = jnp.dot(prev_pnb, first, preferred_element_type=jnp.float32)
        piece_coef = own_coef + passed_along(prev_coef, "dom", -1)
        coef_all = gather_axis(piece_coef, "dom")
        coef = jnp.dot(match, coef_all, precision=lax.Precision.HIGHEST)
        scaled = (couple * coef).astype(jnp.bfloat16)

        neighbour = passed_along(first, "dom", -1)
        kin = jnp.dot(t_own, rounded, preferred_element_type=jnp.float32) + jnp.dot(
            t_nb, neighbour, preferred_element_type=jnp.float32
        )
        cell_out = (kin * srow).reshape(P_SIZE, ROWSP, width)
        hi = cell_out.astype(jnp.bfloat16)
        lo = (cell_out - hi.astype(jnp.float32)).astype(jnp.bfloat16)
        assembled = jnp.einsum("mj,amk->ajk", gs, hi, preferred_element_type=jnp.float32) + jnp.einsum(
            "mj,amk->ajk", gs, lo, preferred_element_type=jnp.float32
        )
        shared = passed_along(assembled[-1], "dom", 1)

        own_part = jnp.einsum("izj,ik->zjk", p_layers, scaled[:pieces], preferred_element_type=jnp.float32)
        prev_part = jnp.dot(prev_pnb.T, scaled[pieces:], preferred_element_type=jnp.float32)
        applied = assembled[:-1] + own_part
        applied = jnp.concatenate([(applied[0] + (shared + prev_part))[None], applied[1:]], axis=0)
        applied = applied.reshape(zl * YXP, width)
        return (applied + shift * current) / halfwidth[0]

    field = jnp.pad(wave.reshape(zl, YX, width), ((0, 0), (0, YXP - YX), (0, 0)))
    previous = field.reshape(zl * YXP, width).astype(jnp.float32)
    current = apply_h(previous)
    for step in range(DEGREE - 1):
        following = 2.0 * apply_h(current) - previous
        previous = current
        current = following
    out = current.reshape(zl, YXP, width)[:, :YX]
    return out.reshape(wave.shape)


def solution(mesh):
    in_specs = (
        P("dom", None, None, "band"),
        P(),
        P("dom"),
        P("dom", None, None),
        P("dom", None),
        P("dom"),
        P("dom"),
        P(),
        P(),
        P(),
    )
    out_specs = P("dom", None, None, "band")
    return jax.shard_map(local, mesh=mesh, in_specs=in_specs, out_specs=out_specs, check_vma=False)
```

```python
import numpy as np
import jax
import jax.numpy as jnp
from jax import lax
from jax.sharding import PartitionSpec as P


P_SIZE = 7
CXC = 2
CYC = 3
CZC = 1
NPROJ = 256
DEGREE = 4

CELLS_DEV = CZC * CYC * CXC
NYN = (P_SIZE - 1) * CYC + 1
NXN = (P_SIZE - 1) * CXC + 1
FACE = P_SIZE * P_SIZE
YX = NYN * NXN
YXP = ((YX + 7) // 8) * 8
ROWS = CELLS_DEV * FACE
ROWSP = ((ROWS + 7) // 8) * 8


def face_gather():
    g = np.zeros((CELLS_DEV, FACE, YXP), np.float32)
    for cy in range(CYC):
        for cx in range(CXC):
            n = cy * CXC + cx
            for b in range(P_SIZE):
                for c in range(P_SIZE):
                    y = (P_SIZE - 1) * cy + b
                    x = (P_SIZE - 1) * cx + c
                    g[n, b * P_SIZE + c, y * NXN + x] = 1.0
    return g


def row_cells():
    idx = np.full((ROWSP,), CELLS_DEV, np.int32)
    idx[:ROWS] = np.repeat(np.arange(CELLS_DEV, dtype=np.int32), FACE)
    return idx


def passed_along(value, axis, steps):
    count = lax.axis_size(axis)
    pairs = [(source, (source + steps) % count) for source in range(count)]
    return lax.ppermute(value, axis, pairs)


def gather_axis(value, axis):
    count = lax.axis_size(axis)
    bit = count // 2
    while bit >= 1:
        pairs = [(source, source ^ bit) for source in range(count)]
        other = lax.ppermute(value, axis, pairs)
        value = jnp.concatenate([value, other], axis=0)
        bit //= 2
    return value


def local(
    wave,
    kinetic,
    cell_scale,
    potential,
    proj_values,
    piece_cell,
    piece_proj,
    coupling,
    center,
    halfwidth,
):
    zl = wave.shape[0]
    width = wave.shape[3]
    pieces = proj_values.shape[0]
    g = jnp.asarray(face_gather(), jnp.bfloat16)

    k4 = kinetic.reshape(P_SIZE, FACE, P_SIZE, FACE)
    t5 = jnp.einsum("pqzb,nbj->pnqzj", k4, g, preferred_element_type=jnp.float32)
    t5 = t5.astype(jnp.bfloat16).reshape(P_SIZE, ROWS, P_SIZE * YXP)
    t5 = jnp.pad(t5, ((0, 0), (0, ROWSP - ROWS), (0, 0)))
    tmat = t5.reshape(P_SIZE * ROWSP, P_SIZE * YXP)
    t_own = tmat[:, : zl * YXP]
    t_nb = tmat[:, zl * YXP :]

    scales = jnp.concatenate([cell_scale, jnp.zeros((1,), jnp.float32)])
    srow = jnp.take(scales, jnp.asarray(row_cells()))
    srow = jnp.tile(srow, P_SIZE)[:, None]

    gs = jnp.pad(g.reshape(ROWS, YXP), ((0, ROWSP - ROWS), (0, 0)))

    sel = (piece_cell[:, None] == jnp.arange(CELLS_DEV, dtype=jnp.int32)[None, :]).astype(jnp.bfloat16)
    gp = jnp.einsum("in,nbj->ibj", sel, g, preferred_element_type=jnp.float32).astype(jnp.bfloat16)
    pv3 = proj_values.reshape(pieces, P_SIZE, FACE)
    pglob = jnp.einsum("izb,ibj->izj", pv3, gp, preferred_element_type=jnp.float32).astype(jnp.bfloat16)
    p_own = pglob[:, :zl].reshape(pieces, zl * YXP)
    p_nb = pglob[:, zl]

    prev_pnb = passed_along(p_nb, "dom", 1)
    ids = jnp.concatenate([piece_proj, passed_along(piece_proj, "dom", 1)])
    ids_row = jnp.zeros((8, width), jnp.float32).at[0, :pieces].set(piece_proj.astype(jnp.float32))
    couple = jnp.take(coupling, ids)[:, None]
    p_layers = pglob[:, :zl]

    pot = jnp.pad(potential.reshape(zl, YX), ((0, 0), (0, YXP - YX)))
    shift = (pot - center[0]).reshape(zl * YXP, 1)

    def apply_h(current, match=None):
        rounded = current.astype(jnp.bfloat16)
        first = rounded[:YXP]
        own_coef = jnp.dot(p_own, rounded, preferred_element_type=jnp.float32)
        prev_coef = jnp.dot(prev_pnb, first, preferred_element_type=jnp.float32)
        piece_coef = own_coef + passed_along(prev_coef, "dom", -1)
        if match is None:
            block = jnp.concatenate([piece_coef, ids_row], axis=0)
            gathered = gather_axis(block, "dom").reshape(-1, pieces + 8, width)
            coef_all = gathered[:, :pieces].reshape(-1, width)
            ids_all = gathered[:, pieces, :pieces].reshape(-1)
            match = (ids.astype(jnp.float32)[:, None] == ids_all[None, :]).astype(jnp.float32)
        else:
            coef_all = gather_axis(piece_coef, "dom")
        coef = jnp.dot(match, coef_all, precision=lax.Precision.HIGHEST)
        scaled = (couple * coef).astype(jnp.bfloat16)

        neighbour = passed_along(first, "dom", -1)
        kin = jnp.dot(t_own, rounded, preferred_element_type=jnp.float32) + jnp.dot(
            t_nb, neighbour, preferred_element_type=jnp.float32
        )
        cell_out = (kin * srow).reshape(P_SIZE, ROWSP, width)
        hi = cell_out.astype(jnp.bfloat16)
        lo = (cell_out - hi.astype(jnp.float32)).astype(jnp.bfloat16)
        assembled = jnp.einsum("mj,amk->ajk", gs, hi, preferred_element_type=jnp.float32) + jnp.einsum(
            "mj,amk->ajk", gs, lo, preferred_element_type=jnp.float32
        )
        shared = passed_along(assembled[-1], "dom", 1)

        own_part = jnp.einsum("izj,ik->zjk", p_layers, scaled[:pieces], preferred_element_type=jnp.float32)
        prev_part = jnp.dot(prev_pnb.T, scaled[pieces:], preferred_element_type=jnp.float32)
        applied = assembled[:-1] + own_part
        applied = jnp.concatenate([(applied[0] + (shared + prev_part))[None], applied[1:]], axis=0)
        applied = applied.reshape(zl * YXP, width)
        return (applied + shift * current) / halfwidth[0], match

    field = jnp.pad(wave.reshape(zl, YX, width), ((0, 0), (0, YXP - YX), (0, 0)))
    previous = field.reshape(zl * YXP, width).astype(jnp.float32)
    current, match = apply_h(previous)
    for step in range(DEGREE - 1):
        following = 2.0 * apply_h(current, match)[0] - previous
        previous = current
        current = following
    out = current.reshape(zl, YXP, width)[:, :YX]
    return out.reshape(wave.shape)


def solution(mesh):
    in_specs = (
        P("dom", None, None, "band"),
        P(),
        P("dom"),
        P("dom", None, None),
        P("dom", None),
        P("dom"),
        P("dom"),
        P(),
        P(),
        P(),
    )
    out_specs = P("dom", None, None, "band")
    return jax.shard_map(local, mesh=mesh, in_specs=in_specs, out_specs=out_specs, check_vma=False)
```

```python
import numpy as np
import jax
import jax.numpy as jnp
from jax import lax
from jax.sharding import PartitionSpec as P


P_SIZE = 7
CXC = 2
CYC = 3
CZC = 1
NPROJ = 256
DEGREE = 4

CELLS_DEV = CZC * CYC * CXC
NYN = (P_SIZE - 1) * CYC + 1
NXN = (P_SIZE - 1) * CXC + 1
FACE = P_SIZE * P_SIZE
YX = NYN * NXN
YXP = ((YX + 7) // 8) * 8
ROWS = CELLS_DEV * FACE
ROWSP = ((ROWS + 7) // 8) * 8


def face_gather():
    g = np.zeros((CELLS_DEV, FACE, YXP), np.float32)
    for cy in range(CYC):
        for cx in range(CXC):
            n = cy * CXC + cx
            for b in range(P_SIZE):
                for c in range(P_SIZE):
                    y = (P_SIZE - 1) * cy + b
                    x = (P_SIZE - 1) * cx + c
                    g[n, b * P_SIZE + c, y * NXN + x] = 1.0
    return g


def row_cells():
    idx = np.full((ROWSP,), CELLS_DEV, np.int32)
    idx[:ROWS] = np.repeat(np.arange(CELLS_DEV, dtype=np.int32), FACE)
    return idx


def passed_along(value, axis, steps):
    count = lax.axis_size(axis)
    pairs = [(source, (source + steps) % count) for source in range(count)]
    return lax.ppermute(value, axis, pairs)


def gather_axis(value, axis):
    count = lax.axis_size(axis)
    bit = count // 2
    while bit >= 1:
        pairs = [(source, source ^ bit) for source in range(count)]
        other = lax.ppermute(value, axis, pairs)
        value = jnp.concatenate([value, other], axis=0)
        bit //= 2
    return value


def local(
    wave,
    kinetic,
    cell_scale,
    potential,
    proj_values,
    piece_cell,
    piece_proj,
    coupling,
    center,
    halfwidth,
):
    zl = wave.shape[0]
    width = wave.shape[3]
    pieces = proj_values.shape[0]
    g = jnp.asarray(face_gather(), jnp.bfloat16)

    scales = jnp.concatenate([cell_scale, jnp.zeros((1,), jnp.float32)])
    srow = jnp.take(scales, jnp.asarray(row_cells()))
    srow = jnp.tile(srow, P_SIZE)[:, None]

    gs = jnp.pad(g.reshape(ROWS, YXP), ((0, ROWSP - ROWS), (0, 0)))

    sel = (piece_cell[:, None] == jnp.arange(CELLS_DEV, dtype=jnp.int32)[None, :]).astype(jnp.bfloat16)
    gp = jnp.einsum("in,nbj->ibj", sel, g, preferred_element_type=jnp.float32).astype(jnp.bfloat16)
    pv3 = proj_values.reshape(pieces, P_SIZE, FACE)
    pglob = jnp.einsum("izb,ibj->izj", pv3, gp, preferred_element_type=jnp.float32).astype(jnp.bfloat16)
    p_own = pglob[:, :zl].reshape(pieces, zl * YXP)
    p_nb = pglob[:, zl]

    prev_pnb = passed_along(p_nb, "dom", 1)
    prev_pnb, kinetic_t = lax.optimization_barrier((prev_pnb, kinetic))

    k4 = kinetic_t.reshape(P_SIZE, FACE, P_SIZE, FACE)
    t5 = jnp.einsum("pqzb,nbj->pnqzj", k4, g, preferred_element_type=jnp.float32)
    t5 = t5.astype(jnp.bfloat16).reshape(P_SIZE, ROWS, P_SIZE * YXP)
    t5 = jnp.pad(t5, ((0, 0), (0, ROWSP - ROWS), (0, 0)))
    tmat = t5.reshape(P_SIZE * ROWSP, P_SIZE * YXP)
    t_own = tmat[:, : zl * YXP]
    t_nb = tmat[:, zl * YXP :]

    ids = jnp.concatenate([piece_proj, passed_along(piece_proj, "dom", 1)])
    ids_row = jnp.zeros((8, width), jnp.float32).at[0, :pieces].set(piece_proj.astype(jnp.float32))
    couple = jnp.take(coupling, ids)[:, None]
    p_layers = pglob[:, :zl]

    pot = jnp.pad(potential.reshape(zl, YX), ((0, 0), (0, YXP - YX)))
    shift = (pot - center[0]).reshape(zl * YXP, 1)

    def apply_h(current, match=None):
        rounded = current.astype(jnp.bfloat16)
        first = rounded[:YXP]
        own_coef = jnp.dot(p_own, rounded, preferred_element_type=jnp.float32)
        prev_coef = jnp.dot(prev_pnb, first, preferred_element_type=jnp.float32)
        piece_coef = own_coef + passed_along(prev_coef, "dom", -1)
        if match is None:
            block = jnp.concatenate([piece_coef, ids_row], axis=0)
            gathered = gather_axis(block, "dom").reshape(-1, pieces + 8, width)
            coef_all = gathered[:, :pieces].reshape(-1, width)
            ids_all = gathered[:, pieces, :pieces].reshape(-1)
            match = (ids.astype(jnp.float32)[:, None] == ids_all[None, :]).astype(jnp.float32)
        else:
            coef_all = gather_axis(piece_coef, "dom")
        coef = jnp.dot(match, coef_all, precision=lax.Precision.HIGHEST)
        scaled = (couple * coef).astype(jnp.bfloat16)

        neighbour = passed_along(first, "dom", -1)
        kin = jnp.dot(t_own, rounded, preferred_element_type=jnp.float32) + jnp.dot(
            t_nb, neighbour, preferred_element_type=jnp.float32
        )
        cell_out = (kin * srow).reshape(P_SIZE, ROWSP, width)
        hi = cell_out.astype(jnp.bfloat16)
        lo = (cell_out - hi.astype(jnp.float32)).astype(jnp.bfloat16)
        assembled = jnp.einsum("mj,amk->ajk", gs, hi, preferred_element_type=jnp.float32) + jnp.einsum(
            "mj,amk->ajk", gs, lo, preferred_element_type=jnp.float32
        )
        shared = passed_along(assembled[-1], "dom", 1)

        own_part = jnp.einsum("izj,ik->zjk", p_layers, scaled[:pieces], preferred_element_type=jnp.float32)
        prev_part = jnp.dot(prev_pnb.T, scaled[pieces:], preferred_element_type=jnp.float32)
        applied = assembled[:-1] + own_part
        applied = jnp.concatenate([(applied[0] + (shared + prev_part))[None], applied[1:]], axis=0)
        applied = applied.reshape(zl * YXP, width)
        return (applied + shift * current) / halfwidth[0], match

    field = jnp.pad(wave.reshape(zl, YX, width), ((0, 0), (0, YXP - YX), (0, 0)))
    previous = field.reshape(zl * YXP, width).astype(jnp.float32)
    current, match = apply_h(previous)
    for step in range(DEGREE - 1):
        following = 2.0 * apply_h(current, match)[0] - previous
        previous = current
        current = following
    out = current.reshape(zl, YXP, width)[:, :YX]
    return out.reshape(wave.shape)


def solution(mesh):
    in_specs = (
        P("dom", None, None, "band"),
        P(),
        P("dom"),
        P("dom", None, None),
        P("dom", None),
        P("dom"),
        P("dom"),
        P(),
        P(),
        P(),
    )
    out_specs = P("dom", None, None, "band")
    return jax.shard_map(local, mesh=mesh, in_specs=in_specs, out_specs=out_specs, check_vma=False)
```

```python
import numpy as np
import jax
import jax.numpy as jnp
from jax import lax
from jax.sharding import PartitionSpec as P


P_SIZE = 7
CXC = 2
CYC = 3
CZC = 1
NPROJ = 256
DEGREE = 4

CELLS_DEV = CZC * CYC * CXC
NYN = (P_SIZE - 1) * CYC + 1
NXN = (P_SIZE - 1) * CXC + 1
FACE = P_SIZE * P_SIZE
YX = NYN * NXN
YXP = ((YX + 7) // 8) * 8
ROWS = CELLS_DEV * FACE
ROWSP = ((ROWS + 7) // 8) * 8


def face_gather():
    g = np.zeros((CELLS_DEV, FACE, YXP), np.float32)
    for cy in range(CYC):
        for cx in range(CXC):
            n = cy * CXC + cx
            for b in range(P_SIZE):
                for c in range(P_SIZE):
                    y = (P_SIZE - 1) * cy + b
                    x = (P_SIZE - 1) * cx + c
                    g[n, b * P_SIZE + c, y * NXN + x] = 1.0
    return g


def row_cells():
    idx = np.full((ROWSP,), CELLS_DEV, np.int32)
    idx[:ROWS] = np.repeat(np.arange(CELLS_DEV, dtype=np.int32), FACE)
    return idx


def passed_along(value, axis, steps):
    count = lax.axis_size(axis)
    pairs = [(source, (source + steps) % count) for source in range(count)]
    return lax.ppermute(value, axis, pairs)


def gather_axis(value, axis):
    count = lax.axis_size(axis)
    bit = count // 2
    while bit >= 1:
        pairs = [(source, source ^ bit) for source in range(count)]
        other = lax.ppermute(value, axis, pairs)
        value = jnp.concatenate([value, other], axis=0)
        bit //= 2
    return value


def local(
    wave,
    kinetic,
    cell_scale,
    potential,
    proj_values,
    piece_cell,
    piece_proj,
    coupling,
    center,
    halfwidth,
):
    zl = wave.shape[0]
    width = wave.shape[3]
    pieces = proj_values.shape[0]
    g = jnp.asarray(face_gather(), jnp.bfloat16)

    scales = jnp.concatenate([cell_scale, jnp.zeros((1,), jnp.float32)])
    srow = jnp.take(scales, jnp.asarray(row_cells()))
    srow = jnp.tile(srow, P_SIZE)[:, None]

    gs = jnp.pad(g.reshape(ROWS, YXP), ((0, ROWSP - ROWS), (0, 0)))

    sel = (piece_cell[:, None] == jnp.arange(CELLS_DEV, dtype=jnp.int32)[None, :]).astype(jnp.bfloat16)
    gp = jnp.einsum("in,nbj->ibj", sel, g, preferred_element_type=jnp.float32).astype(jnp.bfloat16)
    pv3 = proj_values.reshape(pieces, P_SIZE, FACE)
    pglob = jnp.einsum("izb,ibj->izj", pv3, gp, preferred_element_type=jnp.float32).astype(jnp.bfloat16)
    p_own = pglob[:, :zl].reshape(pieces, zl * YXP)
    p_nb = pglob[:, zl]

    prev_pnb = passed_along(p_nb, "dom", 1)
    prev_pnb, kinetic_t = lax.optimization_barrier((prev_pnb, kinetic))

    k4 = kinetic_t.reshape(P_SIZE, FACE, P_SIZE, FACE)
    t5 = jnp.einsum("pqzb,nbj->pnqzj", k4, g, preferred_element_type=jnp.float32)
    t5 = t5.astype(jnp.bfloat16).reshape(P_SIZE, ROWS, P_SIZE * YXP)
    t5 = jnp.pad(t5, ((0, 0), (0, ROWSP - ROWS), (0, 0)))
    tmat = t5.reshape(P_SIZE * ROWSP, P_SIZE * YXP)
    t_own = tmat[:, : zl * YXP]
    t_nb = tmat[:, zl * YXP :]

    ids = jnp.concatenate([piece_proj, passed_along(piece_proj, "dom", 1)])
    ids_row = jnp.zeros((8, width), jnp.bfloat16).at[0, :pieces].set(piece_proj.astype(jnp.bfloat16))
    couple = jnp.take(coupling, ids)[:, None]
    p_layers = pglob[:, :zl]

    pot = jnp.pad(potential.reshape(zl, YX), ((0, 0), (0, YXP - YX)))
    shift = (pot - center[0]).reshape(zl * YXP, 1)

    def apply_h(current, match=None):
        rounded = current.astype(jnp.bfloat16)
        first = rounded[:YXP]
        own_coef = jnp.dot(p_own, rounded, preferred_element_type=jnp.float32)
        prev_coef = jnp.dot(prev_pnb, first, preferred_element_type=jnp.float32)
        piece_coef = own_coef + passed_along(prev_coef.astype(jnp.bfloat16), "dom", -1).astype(jnp.float32)
        piece_coef = piece_coef.astype(jnp.bfloat16)
        if match is None:
            block = jnp.concatenate([piece_coef, ids_row], axis=0)
            gathered = gather_axis(block, "dom").reshape(-1, pieces + 8, width)
            coef_all = gathered[:, :pieces].reshape(-1, width)
            ids_all = gathered[:, pieces, :pieces].reshape(-1)
            match = (ids.astype(jnp.bfloat16)[:, None] == ids_all[None, :]).astype(jnp.bfloat16)
        else:
            coef_all = gather_axis(piece_coef, "dom")
        coef = jnp.dot(match, coef_all, preferred_element_type=jnp.float32)
        scaled = (couple * coef).astype(jnp.bfloat16)

        neighbour = passed_along(first, "dom", -1)
        kin = jnp.dot(t_own, rounded, preferred_element_type=jnp.float32) + jnp.dot(
            t_nb, neighbour, preferred_element_type=jnp.float32
        )
        cell_out = (kin * srow).reshape(P_SIZE, ROWSP, width)
        hi = cell_out.astype(jnp.bfloat16)
        lo = (cell_out - hi.astype(jnp.float32)).astype(jnp.bfloat16)
        assembled = jnp.einsum("mj,amk->ajk", gs, hi, preferred_element_type=jnp.float32) + jnp.einsum(
            "mj,amk->ajk", gs, lo, preferred_element_type=jnp.float32
        )
        shared = passed_along(assembled[-1], "dom", 1)

        own_part = jnp.einsum("izj,ik->zjk", p_layers, scaled[:pieces], preferred_element_type=jnp.float32)
        prev_part = jnp.dot(prev_pnb.T, scaled[pieces:], preferred_element_type=jnp.float32)
        applied = assembled[:-1] + own_part
        applied = jnp.concatenate([(applied[0] + (shared + prev_part))[None], applied[1:]], axis=0)
        applied = applied.reshape(zl * YXP, width)
        return (applied + shift * current) / halfwidth[0], match

    field = jnp.pad(wave.reshape(zl, YX, width), ((0, 0), (0, YXP - YX), (0, 0)))
    previous = field.reshape(zl * YXP, width).astype(jnp.float32)
    current, match = apply_h(previous)
    for step in range(DEGREE - 1):
        following = 2.0 * apply_h(current, match)[0] - previous
        previous = current
        current = following
    out = current.reshape(zl, YXP, width)[:, :YX]
    return out.reshape(wave.shape)


def solution(mesh):
    in_specs = (
        P("dom", None, None, "band"),
        P(),
        P("dom"),
        P("dom", None, None),
        P("dom", None),
        P("dom"),
        P("dom"),
        P(),
        P(),
        P(),
    )
    out_specs = P("dom", None, None, "band")
    return jax.shard_map(local, mesh=mesh, in_specs=in_specs, out_specs=out_specs, check_vma=False)
```

```python
import numpy as np
import jax
import jax.numpy as jnp
from jax import lax
from jax.sharding import PartitionSpec as P


P_SIZE = 7
CXC = 2
CYC = 3
CZC = 1
NPROJ = 256
DEGREE = 4

CELLS_DEV = CZC * CYC * CXC
NYN = (P_SIZE - 1) * CYC + 1
NXN = (P_SIZE - 1) * CXC + 1
FACE = P_SIZE * P_SIZE
YX = NYN * NXN
YXP = ((YX + 7) // 8) * 8
ROWS = CELLS_DEV * FACE
ROWSP = ((ROWS + 7) // 8) * 8


def face_gather():
    g = np.zeros((CELLS_DEV, FACE, YXP), np.float32)
    for cy in range(CYC):
        for cx in range(CXC):
            n = cy * CXC + cx
            for b in range(P_SIZE):
                for c in range(P_SIZE):
                    y = (P_SIZE - 1) * cy + b
                    x = (P_SIZE - 1) * cx + c
                    g[n, b * P_SIZE + c, y * NXN + x] = 1.0
    return g


def row_cells():
    idx = np.full((ROWSP,), CELLS_DEV, np.int32)
    idx[:ROWS] = np.repeat(np.arange(CELLS_DEV, dtype=np.int32), FACE)
    return idx


def passed_along(value, axis, steps):
    count = lax.axis_size(axis)
    pairs = [(source, (source + steps) % count) for source in range(count)]
    return lax.ppermute(value, axis, pairs)


def gather_axis(value, axis):
    count = lax.axis_size(axis)
    bit = count // 2
    while bit >= 1:
        pairs = [(source, source ^ bit) for source in range(count)]
        other = lax.ppermute(value, axis, pairs)
        value = jnp.concatenate([value, other], axis=0)
        bit //= 2
    return value


def local(
    wave,
    kinetic,
    cell_scale,
    potential,
    proj_values,
    piece_cell,
    piece_proj,
    coupling,
    center,
    halfwidth,
):
    zl = wave.shape[0]
    width = wave.shape[3]
    pieces = proj_values.shape[0]
    g = jnp.asarray(face_gather(), jnp.bfloat16)

    scales = jnp.concatenate([cell_scale, jnp.zeros((1,), jnp.float32)])
    srow = jnp.take(scales, jnp.asarray(row_cells()))
    srow = jnp.tile(srow, P_SIZE)[:, None]

    gs = jnp.pad(g.reshape(ROWS, YXP), ((0, ROWSP - ROWS), (0, 0)))

    sel = (piece_cell[:, None] == jnp.arange(CELLS_DEV, dtype=jnp.int32)[None, :]).astype(jnp.bfloat16)
    gp = jnp.einsum("in,nbj->ibj", sel, g, preferred_element_type=jnp.float32).astype(jnp.bfloat16)
    pv3 = proj_values.reshape(pieces, P_SIZE, FACE)
    pglob = jnp.einsum("izb,ibj->izj", pv3, gp, preferred_element_type=jnp.float32).astype(jnp.bfloat16)
    p_own = pglob[:, :zl].reshape(pieces, zl * YXP)
    p_nb = pglob[:, zl]

    prev_pnb = passed_along(p_nb, "dom", 1)
    prev_pnb, kinetic_t = lax.optimization_barrier((prev_pnb, kinetic))

    k4 = kinetic_t.reshape(P_SIZE, FACE, P_SIZE, FACE)
    t5 = jnp.einsum("pqzb,nbj->pnqzj", k4, g, preferred_element_type=jnp.float32)
    t5 = t5.astype(jnp.bfloat16).reshape(P_SIZE, ROWS, P_SIZE * YXP)
    t5 = jnp.pad(t5, ((0, 0), (0, ROWSP - ROWS), (0, 0)))
    tmat = t5.reshape(P_SIZE * ROWSP, P_SIZE * YXP)
    t_own = tmat[:, : zl * YXP]
    t_nb = tmat[:, zl * YXP :]

    ids = jnp.concatenate([piece_proj, passed_along(piece_proj, "dom", 1)])
    ids_row = jnp.zeros((8, width), jnp.bfloat16).at[0, :pieces].set(piece_proj.astype(jnp.bfloat16))
    couple = jnp.take(coupling, ids)[:, None]
    p_layers = pglob[:, :zl]

    pot = jnp.pad(potential.reshape(zl, YX), ((0, 0), (0, YXP - YX)))
    shift = (pot - center[0]).reshape(zl * YXP, 1)

    def apply_h(current, match=None):
        rounded = current.astype(jnp.bfloat16)
        first = rounded[:YXP]
        own_coef = jnp.dot(p_own, rounded, preferred_element_type=jnp.float32)
        prev_coef = jnp.dot(prev_pnb, first, preferred_element_type=jnp.float32)
        prev_recv = passed_along(prev_coef.astype(jnp.bfloat16), "dom", -1)
        rounded_k, prev_recv = lax.optimization_barrier((rounded, prev_recv))
        piece_coef = own_coef + prev_recv.astype(jnp.float32)
        piece_coef = piece_coef.astype(jnp.bfloat16)
        if match is None:
            block = jnp.concatenate([piece_coef, ids_row], axis=0)
            gathered = gather_axis(block, "dom").reshape(-1, pieces + 8, width)
            coef_all = gathered[:, :pieces].reshape(-1, width)
            ids_all = gathered[:, pieces, :pieces].reshape(-1)
            match = (ids.astype(jnp.bfloat16)[:, None] == ids_all[None, :]).astype(jnp.bfloat16)
        else:
            coef_all = gather_axis(piece_coef, "dom")
        coef = jnp.dot(match, coef_all, preferred_element_type=jnp.float32)
        scaled = (couple * coef).astype(jnp.bfloat16)

        neighbour = passed_along(first, "dom", -1)
        kin = jnp.dot(t_own, rounded_k, preferred_element_type=jnp.float32) + jnp.dot(
            t_nb, neighbour, preferred_element_type=jnp.float32
        )
        cell_out = (kin * srow).reshape(P_SIZE, ROWSP, width)
        hi = cell_out.astype(jnp.bfloat16)
        lo = (cell_out - hi.astype(jnp.float32)).astype(jnp.bfloat16)
        assembled = jnp.einsum("mj,amk->ajk", gs, hi, preferred_element_type=jnp.float32) + jnp.einsum(
            "mj,amk->ajk", gs, lo, preferred_element_type=jnp.float32
        )
        shared = passed_along(assembled[-1], "dom", 1)

        own_part = jnp.einsum("izj,ik->zjk", p_layers, scaled[:pieces], preferred_element_type=jnp.float32)
        prev_part = jnp.dot(prev_pnb.T, scaled[pieces:], preferred_element_type=jnp.float32)
        applied = assembled[:-1] + own_part
        applied = jnp.concatenate([(applied[0] + (shared + prev_part))[None], applied[1:]], axis=0)
        applied = applied.reshape(zl * YXP, width)
        return (applied + shift * current) / halfwidth[0], match

    field = jnp.pad(wave.reshape(zl, YX, width), ((0, 0), (0, YXP - YX), (0, 0)))
    previous = field.reshape(zl * YXP, width).astype(jnp.float32)
    current, match = apply_h(previous)
    for step in range(DEGREE - 1):
        following = 2.0 * apply_h(current, match)[0] - previous
        previous = current
        current = following
    out = current.reshape(zl, YXP, width)[:, :YX]
    return out.reshape(wave.shape)


def solution(mesh):
    in_specs = (
        P("dom", None, None, "band"),
        P(),
        P("dom"),
        P("dom", None, None),
        P("dom", None),
        P("dom"),
        P("dom"),
        P(),
        P(),
        P(),
    )
    out_specs = P("dom", None, None, "band")
    return jax.shard_map(local, mesh=mesh, in_specs=in_specs, out_specs=out_specs, check_vma=False)
```

```python
import numpy as np
import jax
import jax.numpy as jnp
from jax import lax
from jax.sharding import PartitionSpec as P


P_SIZE = 7
CXC = 2
CYC = 3
CZC = 1
NPROJ = 256
DEGREE = 4

CELLS_DEV = CZC * CYC * CXC
NYN = (P_SIZE - 1) * CYC + 1
NXN = (P_SIZE - 1) * CXC + 1
FACE = P_SIZE * P_SIZE
YX = NYN * NXN
YXP = ((YX + 7) // 8) * 8
ROWS = CELLS_DEV * FACE
ROWSP = ((ROWS + 7) // 8) * 8


def face_gather():
    g = np.zeros((CELLS_DEV, FACE, YXP), np.float32)
    for cy in range(CYC):
        for cx in range(CXC):
            n = cy * CXC + cx
            for b in range(P_SIZE):
                for c in range(P_SIZE):
                    y = (P_SIZE - 1) * cy + b
                    x = (P_SIZE - 1) * cx + c
                    g[n, b * P_SIZE + c, y * NXN + x] = 1.0
    return g


def row_cells():
    idx = np.full((ROWSP,), CELLS_DEV, np.int32)
    idx[:ROWS] = np.repeat(np.arange(CELLS_DEV, dtype=np.int32), FACE)
    return idx


def passed_along(value, axis, steps):
    count = lax.axis_size(axis)
    pairs = [(source, (source + steps) % count) for source in range(count)]
    return lax.ppermute(value, axis, pairs)


def gather_axis(value, axis, tie):
    count = lax.axis_size(axis)
    bit = count // 2
    while bit >= 1:
        if bit == count // 8:
            value, tie = lax.optimization_barrier((value, tie))
        pairs = [(source, source ^ bit) for source in range(count)]
        other = lax.ppermute(value, axis, pairs)
        value = jnp.concatenate([value, other], axis=0)
        bit //= 2
    return value, tie


def local(
    wave,
    kinetic,
    cell_scale,
    potential,
    proj_values,
    piece_cell,
    piece_proj,
    coupling,
    center,
    halfwidth,
):
    zl = wave.shape[0]
    width = wave.shape[3]
    pieces = proj_values.shape[0]
    g = jnp.asarray(face_gather(), jnp.bfloat16)

    scales = jnp.concatenate([cell_scale, jnp.zeros((1,), jnp.float32)])
    srow = jnp.take(scales, jnp.asarray(row_cells()))
    srow = jnp.tile(srow, P_SIZE)[:, None]

    gs = jnp.pad(g.reshape(ROWS, YXP), ((0, ROWSP - ROWS), (0, 0)))

    sel = (piece_cell[:, None] == jnp.arange(CELLS_DEV, dtype=jnp.int32)[None, :]).astype(jnp.bfloat16)
    gp = jnp.einsum("in,nbj->ibj", sel, g, preferred_element_type=jnp.float32).astype(jnp.bfloat16)
    pv3 = proj_values.reshape(pieces, P_SIZE, FACE)
    pglob = jnp.einsum("izb,ibj->izj", pv3, gp, preferred_element_type=jnp.float32).astype(jnp.bfloat16)
    p_own = pglob[:, :zl].reshape(pieces, zl * YXP)
    p_nb = pglob[:, zl]

    prev_pnb = passed_along(p_nb, "dom", 1)
    prev_pnb, kinetic_t = lax.optimization_barrier((prev_pnb, kinetic))

    k4 = kinetic_t.reshape(P_SIZE, FACE, P_SIZE, FACE)
    t5 = jnp.einsum("pqzb,nbj->pnqzj", k4, g, preferred_element_type=jnp.float32)
    t5 = t5.astype(jnp.bfloat16).reshape(P_SIZE, ROWS, P_SIZE * YXP)
    t5 = jnp.pad(t5, ((0, 0), (0, ROWSP - ROWS), (0, 0)))
    tmat = t5.reshape(P_SIZE * ROWSP, P_SIZE * YXP)
    t_own = tmat[:, : zl * YXP]
    t_nb = tmat[:, zl * YXP :]

    ids = jnp.concatenate([piece_proj, passed_along(piece_proj, "dom", 1)])
    ids_row = jnp.zeros((8, width), jnp.bfloat16).at[0, :pieces].set(piece_proj.astype(jnp.bfloat16))
    couple = jnp.take(coupling, ids)[:, None]
    p_layers = pglob[:, :zl]

    pot = jnp.pad(potential.reshape(zl, YX), ((0, 0), (0, YXP - YX)))
    shift = (pot - center[0]).reshape(zl * YXP, 1)

    def apply_h(current, match=None):
        rounded = current.astype(jnp.bfloat16)
        first = rounded[:YXP]
        own_coef = jnp.dot(p_own, rounded, preferred_element_type=jnp.float32)
        prev_coef = jnp.dot(prev_pnb, first, preferred_element_type=jnp.float32)
        prev_recv = passed_along(prev_coef.astype(jnp.bfloat16), "dom", -1)
        rounded_k, prev_recv = lax.optimization_barrier((rounded, prev_recv))
        piece_coef = own_coef + prev_recv.astype(jnp.float32)
        piece_coef = piece_coef.astype(jnp.bfloat16)
        neighbour = passed_along(first, "dom", -1)

        def assemble(rows):
            kin = jnp.dot(t_own[rows], rounded_k, preferred_element_type=jnp.float32) + jnp.dot(
                t_nb[rows], neighbour, preferred_element_type=jnp.float32
            )
            cell_out = (kin * srow[rows]).reshape(-1, ROWSP, width)
            hi = cell_out.astype(jnp.bfloat16)
            lo = (cell_out - hi.astype(jnp.float32)).astype(jnp.bfloat16)
            return jnp.einsum("mj,amk->ajk", gs, hi, preferred_element_type=jnp.float32) + jnp.einsum(
                "mj,amk->ajk", gs, lo, preferred_element_type=jnp.float32
            )

        top = assemble(slice(zl * ROWSP, None))
        shared = passed_along(top[0], "dom", 1)

        if match is None:
            block = jnp.concatenate([piece_coef, ids_row], axis=0)
            gathered, shared = gather_axis(block, "dom", shared)
            gathered = gathered.reshape(-1, pieces + 8, width)
            coef_all = gathered[:, :pieces].reshape(-1, width)
            ids_all = gathered[:, pieces, :pieces].reshape(-1)
            match = (ids.astype(jnp.bfloat16)[:, None] == ids_all[None, :]).astype(jnp.bfloat16)
        else:
            coef_all, shared = gather_axis(piece_coef, "dom", shared)
        coef = jnp.dot(match, coef_all, preferred_element_type=jnp.float32)
        scaled = (couple * coef).astype(jnp.bfloat16)

        assembled = assemble(slice(None, zl * ROWSP))

        own_part = jnp.einsum("izj,ik->zjk", p_layers, scaled[:pieces], preferred_element_type=jnp.float32)
        prev_part = jnp.dot(prev_pnb.T, scaled[pieces:], preferred_element_type=jnp.float32)
        applied = assembled + own_part
        applied = jnp.concatenate([(applied[0] + (shared + prev_part))[None], applied[1:]], axis=0)
        applied = applied.reshape(zl * YXP, width)
        return (applied + shift * current) / halfwidth[0], match

    field = jnp.pad(wave.reshape(zl, YX, width), ((0, 0), (0, YXP - YX), (0, 0)))
    previous = field.reshape(zl * YXP, width).astype(jnp.float32)
    current, match = apply_h(previous)
    for step in range(DEGREE - 1):
        following = 2.0 * apply_h(current, match)[0] - previous
        previous = current
        current = following
    out = current.reshape(zl, YXP, width)[:, :YX]
    return out.reshape(wave.shape)


def solution(mesh):
    in_specs = (
        P("dom", None, None, "band"),
        P(),
        P("dom"),
        P("dom", None, None),
        P("dom", None),
        P("dom"),
        P("dom"),
        P(),
        P(),
        P(),
    )
    out_specs = P("dom", None, None, "band")
    return jax.shard_map(local, mesh=mesh, in_specs=in_specs, out_specs=out_specs, check_vma=False)
```

```python
import numpy as np
import jax
import jax.numpy as jnp
from jax import lax
from jax.sharding import PartitionSpec as P


P_SIZE = 7
CXC = 2
CYC = 3
CZC = 1
NPROJ = 256
DEGREE = 4

CELLS_DEV = CZC * CYC * CXC
NYN = (P_SIZE - 1) * CYC + 1
NXN = (P_SIZE - 1) * CXC + 1
FACE = P_SIZE * P_SIZE
YX = NYN * NXN
YXP = ((YX + 7) // 8) * 8
ROWS = CELLS_DEV * FACE
ROWSP = ((ROWS + 7) // 8) * 8


def face_gather():
    g = np.zeros((CELLS_DEV, FACE, YXP), np.float32)
    for cy in range(CYC):
        for cx in range(CXC):
            n = cy * CXC + cx
            for b in range(P_SIZE):
                for c in range(P_SIZE):
                    y = (P_SIZE - 1) * cy + b
                    x = (P_SIZE - 1) * cx + c
                    g[n, b * P_SIZE + c, y * NXN + x] = 1.0
    return g


def row_cells():
    idx = np.full((ROWSP,), CELLS_DEV, np.int32)
    idx[:ROWS] = np.repeat(np.arange(CELLS_DEV, dtype=np.int32), FACE)
    return idx


def passed_along(value, axis, steps):
    count = lax.axis_size(axis)
    pairs = [(source, (source + steps) % count) for source in range(count)]
    return lax.ppermute(value, axis, pairs)


def gather_axis(value, axis, tie):
    count = lax.axis_size(axis)
    bit = count // 2
    while bit >= 1:
        pairs = [(source, source ^ bit) for source in range(count)]
        other = lax.ppermute(value, axis, pairs)
        value = jnp.concatenate([value, other], axis=0)
        bit //= 2
    return value, tie


def local(
    wave,
    kinetic,
    cell_scale,
    potential,
    proj_values,
    piece_cell,
    piece_proj,
    coupling,
    center,
    halfwidth,
):
    zl = wave.shape[0]
    width = wave.shape[3]
    pieces = proj_values.shape[0]
    g = jnp.asarray(face_gather(), jnp.bfloat16)

    scales = jnp.concatenate([cell_scale, jnp.zeros((1,), jnp.float32)])
    srow = jnp.take(scales, jnp.asarray(row_cells()))
    srow = jnp.tile(srow, P_SIZE)[:, None]

    gs = jnp.pad(g.reshape(ROWS, YXP), ((0, ROWSP - ROWS), (0, 0)))

    sel = (piece_cell[:, None] == jnp.arange(CELLS_DEV, dtype=jnp.int32)[None, :]).astype(jnp.bfloat16)
    gp = jnp.einsum("in,nbj->ibj", sel, g, preferred_element_type=jnp.float32).astype(jnp.bfloat16)
    pv3 = proj_values.reshape(pieces, P_SIZE, FACE)
    pglob = jnp.einsum("izb,ibj->izj", pv3, gp, preferred_element_type=jnp.float32).astype(jnp.bfloat16)
    p_own = pglob[:, :zl].reshape(pieces, zl * YXP)
    p_nb = pglob[:, zl]

    prev_pnb = passed_along(p_nb, "dom", 1)
    prev_pnb, kinetic_t = lax.optimization_barrier((prev_pnb, kinetic))

    k4 = kinetic_t.reshape(P_SIZE, FACE, P_SIZE, FACE)
    t5 = jnp.einsum("pqzb,nbj->pnqzj", k4, g, preferred_element_type=jnp.float32)
    t5 = t5.astype(jnp.bfloat16).reshape(P_SIZE, ROWS, P_SIZE * YXP)
    t5 = jnp.pad(t5, ((0, 0), (0, ROWSP - ROWS), (0, 0)))
    tmat = t5.reshape(P_SIZE * ROWSP, P_SIZE * YXP)
    t_own = tmat[:, : zl * YXP]
    t_nb = tmat[:, zl * YXP :]

    ids = jnp.concatenate([piece_proj, passed_along(piece_proj, "dom", 1)])
    ids_row = jnp.zeros((8, width), jnp.bfloat16).at[0, :pieces].set(piece_proj.astype(jnp.bfloat16))
    couple = jnp.take(coupling, ids)[:, None]
    p_layers = pglob[:, :zl]

    pot = jnp.pad(potential.reshape(zl, YX), ((0, 0), (0, YXP - YX)))
    shift = (pot - center[0]).reshape(zl * YXP, 1)

    def apply_h(current, match=None):
        rounded = current.astype(jnp.bfloat16)
        first = rounded[:YXP]
        own_coef = jnp.dot(p_own, rounded, preferred_element_type=jnp.float32)
        prev_coef = jnp.dot(prev_pnb, first, preferred_element_type=jnp.float32)
        prev_recv = passed_along(prev_coef.astype(jnp.bfloat16), "dom", -1)
        rounded_k, prev_recv = lax.optimization_barrier((rounded, prev_recv))
        piece_coef = own_coef + prev_recv.astype(jnp.float32)
        piece_coef = piece_coef.astype(jnp.bfloat16)
        neighbour = passed_along(first, "dom", -1)

        def assemble(rows):
            kin = jnp.dot(t_own[rows], rounded_k, preferred_element_type=jnp.float32) + jnp.dot(
                t_nb[rows], neighbour, preferred_element_type=jnp.float32
            )
            cell_out = (kin * srow[rows]).reshape(-1, ROWSP, width)
            hi = cell_out.astype(jnp.bfloat16)
            lo = (cell_out - hi.astype(jnp.float32)).astype(jnp.bfloat16)
            return jnp.einsum("mj,amk->ajk", gs, hi, preferred_element_type=jnp.float32) + jnp.einsum(
                "mj,amk->ajk", gs, lo, preferred_element_type=jnp.float32
            )

        top = assemble(slice(zl * ROWSP, None))
        shared = passed_along(top[0], "dom", 1)

        if match is None:
            block = jnp.concatenate([piece_coef, ids_row], axis=0)
            gathered, shared = gather_axis(block, "dom", shared)
            gathered = gathered.reshape(-1, pieces + 8, width)
            coef_all = gathered[:, :pieces].reshape(-1, width)
            ids_all = gathered[:, pieces, :pieces].reshape(-1)
            match = (ids.astype(jnp.bfloat16)[:, None] == ids_all[None, :]).astype(jnp.bfloat16)
        else:
            coef_all, shared = gather_axis(piece_coef, "dom", shared)
        coef = jnp.dot(match, coef_all, preferred_element_type=jnp.float32)
        scaled = (couple * coef).astype(jnp.bfloat16)

        assembled = assemble(slice(None, zl * ROWSP))

        own_part = jnp.einsum("izj,ik->zjk", p_layers, scaled[:pieces], preferred_element_type=jnp.float32)
        prev_part = jnp.dot(prev_pnb.T, scaled[pieces:], preferred_element_type=jnp.float32)
        applied = assembled + own_part
        applied = jnp.concatenate([(applied[0] + (shared + prev_part))[None], applied[1:]], axis=0)
        applied = applied.reshape(zl * YXP, width)
        return (applied + shift * current) / halfwidth[0], match

    field = jnp.pad(wave.reshape(zl, YX, width), ((0, 0), (0, YXP - YX), (0, 0)))
    previous = field.reshape(zl * YXP, width).astype(jnp.float32)
    current, match = apply_h(previous)
    for step in range(DEGREE - 1):
        following = 2.0 * apply_h(current, match)[0] - previous
        previous = current
        current = following
    out = current.reshape(zl, YXP, width)[:, :YX]
    return out.reshape(wave.shape)


def solution(mesh):
    in_specs = (
        P("dom", None, None, "band"),
        P(),
        P("dom"),
        P("dom", None, None),
        P("dom", None),
        P("dom"),
        P("dom"),
        P(),
        P(),
        P(),
    )
    out_specs = P("dom", None, None, "band")
    return jax.shard_map(local, mesh=mesh, in_specs=in_specs, out_specs=out_specs, check_vma=False)
```

```python
import numpy as np
import jax
import jax.numpy as jnp
from jax import lax
from jax.sharding import PartitionSpec as P


P_SIZE = 7
CXC = 2
CYC = 3
CZC = 1
NPROJ = 256
DEGREE = 4

CELLS_DEV = CZC * CYC * CXC
NYN = (P_SIZE - 1) * CYC + 1
NXN = (P_SIZE - 1) * CXC + 1
FACE = P_SIZE * P_SIZE
YX = NYN * NXN
YXP = ((YX + 7) // 8) * 8
ROWS = CELLS_DEV * FACE
ROWSP = ((ROWS + 7) // 8) * 8


def face_gather():
    g = np.zeros((CELLS_DEV, FACE, YXP), np.float32)
    for cy in range(CYC):
        for cx in range(CXC):
            n = cy * CXC + cx
            for b in range(P_SIZE):
                for c in range(P_SIZE):
                    y = (P_SIZE - 1) * cy + b
                    x = (P_SIZE - 1) * cx + c
                    g[n, b * P_SIZE + c, y * NXN + x] = 1.0
    return g


def row_cells():
    idx = np.full((ROWSP,), CELLS_DEV, np.int32)
    idx[:ROWS] = np.repeat(np.arange(CELLS_DEV, dtype=np.int32), FACE)
    return idx


def passed_along(value, axis, steps):
    count = lax.axis_size(axis)
    pairs = [(source, (source + steps) % count) for source in range(count)]
    return lax.ppermute(value, axis, pairs)


def gather_axis(value, axis):
    count = lax.axis_size(axis)
    bit = count // 2
    while bit >= 1:
        pairs = [(source, source ^ bit) for source in range(count)]
        other = lax.ppermute(value, axis, pairs)
        value = jnp.concatenate([value, other], axis=0)
        bit //= 2
    return value


def local(
    wave,
    kinetic,
    cell_scale,
    potential,
    proj_values,
    piece_cell,
    piece_proj,
    coupling,
    center,
    halfwidth,
):
    zl = wave.shape[0]
    width = wave.shape[3]
    pieces = proj_values.shape[0]
    g = jnp.asarray(face_gather(), jnp.bfloat16)

    scales = jnp.concatenate([cell_scale, jnp.zeros((1,), jnp.float32)])
    srow = jnp.take(scales, jnp.asarray(row_cells()))
    srow = jnp.tile(srow, P_SIZE)[:, None]

    gs = jnp.pad(g.reshape(ROWS, YXP), ((0, ROWSP - ROWS), (0, 0)))

    sel = (piece_cell[:, None] == jnp.arange(CELLS_DEV, dtype=jnp.int32)[None, :]).astype(jnp.bfloat16)
    gp = jnp.einsum("in,nbj->ibj", sel, g, preferred_element_type=jnp.float32).astype(jnp.bfloat16)
    pv3 = proj_values.reshape(pieces, P_SIZE, FACE)
    pglob = jnp.einsum("izb,ibj->izj", pv3, gp, preferred_element_type=jnp.float32).astype(jnp.bfloat16)
    p_own = pglob[:, :zl].reshape(pieces, zl * YXP)
    p_nb = pglob[:, zl]

    prev_pnb = passed_along(p_nb, "dom", 1)
    prev_pnb, kinetic_t = lax.optimization_barrier((prev_pnb, kinetic))

    k4 = kinetic_t.reshape(P_SIZE, FACE, P_SIZE, FACE)
    t5 = jnp.einsum("pqzb,nbj->pnqzj", k4, g, preferred_element_type=jnp.float32)
    t5 = t5.astype(jnp.bfloat16).reshape(P_SIZE, ROWS, P_SIZE * YXP)
    t5 = jnp.pad(t5, ((0, 0), (0, ROWSP - ROWS), (0, 0)))
    tmat = t5.reshape(P_SIZE * ROWSP, P_SIZE * YXP)
    t_own = tmat[:, : zl * YXP]
    t_nb = tmat[:, zl * YXP :]

    ids = jnp.concatenate([piece_proj, passed_along(piece_proj, "dom", 1)])
    ids_row = jnp.zeros((8, width), jnp.bfloat16).at[0, :pieces].set(piece_proj.astype(jnp.bfloat16))
    couple = jnp.take(coupling, ids)[:, None]
    p_layers = pglob[:, :zl]

    pot = jnp.pad(potential.reshape(zl, YX), ((0, 0), (0, YXP - YX)))
    shift = (pot - center[0]).reshape(zl * YXP, 1)

    def apply_h(current, match=None):
        rounded = current.astype(jnp.bfloat16)
        first = rounded[:YXP]
        own_coef = jnp.dot(p_own, rounded, preferred_element_type=jnp.float32)
        prev_coef = jnp.dot(prev_pnb, first, preferred_element_type=jnp.float32)
        prev_recv = passed_along(prev_coef.astype(jnp.bfloat16), "dom", -1)
        rounded_k, prev_recv = lax.optimization_barrier((rounded, prev_recv))
        piece_coef = own_coef + prev_recv.astype(jnp.float32)
        piece_coef = piece_coef.astype(jnp.bfloat16)
        if match is None:
            block = jnp.concatenate([piece_coef, ids_row], axis=0)
            gathered = gather_axis(block, "dom").reshape(-1, pieces + 8, width)
            coef_all = gathered[:, :pieces].reshape(-1, width)
            ids_all = gathered[:, pieces, :pieces].reshape(-1)
            match = (ids.astype(jnp.bfloat16)[:, None] == ids_all[None, :]).astype(jnp.bfloat16)
        else:
            coef_all = gather_axis(piece_coef, "dom")
        coef = jnp.dot(match, coef_all, preferred_element_type=jnp.float32)
        scaled = (couple * coef).astype(jnp.bfloat16)

        neighbour = passed_along(first, "dom", -1)
        kin = jnp.dot(t_own, rounded_k, preferred_element_type=jnp.float32) + jnp.dot(
            t_nb, neighbour, preferred_element_type=jnp.float32
        )
        cell_out = (kin * srow).reshape(P_SIZE, ROWSP, width)
        hi = cell_out.astype(jnp.bfloat16)
        lo = (cell_out - hi.astype(jnp.float32)).astype(jnp.bfloat16)
        both = jnp.einsum("mj,amk->ajk", gs, jnp.concatenate([hi, lo], axis=-1), preferred_element_type=jnp.float32)
        assembled = both[..., :width] + both[..., width:]
        shared = passed_along(assembled[-1], "dom", 1)

        own_part = jnp.einsum("izj,ik->zjk", p_layers, scaled[:pieces], preferred_element_type=jnp.float32)
        prev_part = jnp.dot(prev_pnb.T, scaled[pieces:], preferred_element_type=jnp.float32)
        applied = assembled[:-1] + own_part
        applied = jnp.concatenate([(applied[0] + (shared + prev_part))[None], applied[1:]], axis=0)
        applied = applied.reshape(zl * YXP, width)
        return (applied + shift * current) / halfwidth[0], match

    field = jnp.pad(wave.reshape(zl, YX, width), ((0, 0), (0, YXP - YX), (0, 0)))
    previous = field.reshape(zl * YXP, width).astype(jnp.float32)
    current, match = apply_h(previous)
    for step in range(DEGREE - 1):
        following = 2.0 * apply_h(current, match)[0] - previous
        previous = current
        current = following
    out = current.reshape(zl, YXP, width)[:, :YX]
    return out.reshape(wave.shape)


def solution(mesh):
    in_specs = (
        P("dom", None, None, "band"),
        P(),
        P("dom"),
        P("dom", None, None),
        P("dom", None),
        P("dom"),
        P("dom"),
        P(),
        P(),
        P(),
    )
    out_specs = P("dom", None, None, "band")
    return jax.shard_map(local, mesh=mesh, in_specs=in_specs, out_specs=out_specs, check_vma=False)
```
